128 devices in a mesh: gx: 16 (over z, y), gy: 8 (over x, core).
Axes of the slice: x: 4, y: 4, z: 4, core: 2. Of those that a mesh axis runs over, the one named last changes fastest.
Arguments:
- tile_sums: bfloat16 [16384, 5, 16384], P(('gx', 'gy')), may hold values from -180 to 180
- tile_dest: int32 [16384], P(('gx', 'gy')), may hold values from 0 to 127, as said below
- tile_place: int32 [16384], P(('gx', 'gy')), may hold values from 0 to 15
- tile_count: int32 [128], P(('gx', 'gy')), may hold values from 64 to 128, as said below
Outputs:
- smoothed: float32 [5, 16, 1024, 2048], P(None, 'gx', 'gy')
The draws below stay inside these ranges and needn't reach their ends.
Inputs may be any that keep to these rules, and one draw needn't show every extreme that they name: `tile_dest`: each DEM device's 128 records name every filter device exactly once. Only the first tile_count[d] slots of device d are live; some device has all 128 live and some has half.
All inputs are finite; a program needn't handle non-finite values.
Results may differ from the reference program's by a relative error of at most 0.0003.
Values may be sent and summed in bfloat16 or wider, within the bound.
No kernel may reach another device: no remote copies, remote signals or barrier semaphores. Data moves between devices by JAX's collectives and lax.ppermute only.
A program may use at most 192 MiB of HBM per device.

```python
import math
import jax
import jax.numpy as jnp
from jax import lax

NF = 5
TE = 32
BX = 4
BY = 4
RADIUS = 4
NZ = 16
TCELLS = 16384
SLOTS = 128
RECORDS = 16384
N_GX = 16
N_GY = 8
DEVICES = 128


def draw_tile_dest(key, part):
    score_key, favour_key = jax.random.split(jax.random.fold_in(key, 11))
    columns = jnp.arange(DEVICES, dtype=jnp.int32)
    scores = jax.random.randint(score_key, (DEVICES, DEVICES), 0, 65536, dtype=jnp.int32) * DEVICES + columns[None, :]
    favour = jax.random.randint(favour_key, (DEVICES,), 0, 4, dtype=jnp.int32) * (16384 * DEVICES)
    ranked = jnp.argsort(-(scores + favour[None, :]), axis=1, stable=True)
    return ranked[:, :SLOTS].reshape(DEVICES * SLOTS).astype(jnp.int32)


def draw_tile_count(key, part):
    first_key, second_key, third_key = jax.random.split(jax.random.fold_in(key, 23), 3)
    counts = jax.random.randint(first_key, (DEVICES,), SLOTS // 2, SLOTS + 1, dtype=jnp.int32)
    fullest = jax.random.randint(second_key, (), 0, DEVICES, dtype=jnp.int32)
    emptiest = (fullest + 1 + jax.random.randint(third_key, (), 0, DEVICES - 1, dtype=jnp.int32)) % DEVICES
    positions = jnp.arange(DEVICES, dtype=jnp.int32)
    counts = jnp.where(positions == fullest, SLOTS, counts)
    counts = jnp.where(positions == emptiest, SLOTS // 2, counts)
    return counts.astype(jnp.int32)


def touch_ends(array, key, smallest, high):
    longest = array.shape.index(max(array.shape))
    spots = []
    for shift in (0, 1):
        where = [jax.random.randint(jax.random.fold_in(key, axis), (), 0, length) for axis, length in enumerate(array.shape)]
        where[longest] = (where[longest] + shift) % array.shape[longest]
        spots.append(tuple(where))
    return array.at[spots[0]].set(smallest).at[spots[1]].set(high)


def block_levels(rng, dims, pieces, low, largest):
    gain = 1.0
    for dim, shards_of in pieces:
        heights = jax.random.uniform(jax.random.fold_in(jax.random.fold_in(rng, 6), dim), (shards_of,), jnp.float32, low / len(pieces), largest / len(pieces))
        gain = gain * jnp.repeat(jnp.exp(heights), dims[dim] // shards_of).reshape((-1,) + (1,) * (len(dims) - 1 - dim))
    return gain


def gaussian(rng, extent, scale, reach, cuts=(), kind=jnp.bfloat16):
    loudness = block_levels(rng, extent, cuts, -0.22, 0.18) if cuts else 1.0
    entries = jax.random.normal(rng, extent, jnp.float32) * scale * loudness
    return jnp.minimum(jnp.maximum(entries, -reach), reach).astype(kind)


def setup_inputs(seed: int = 0) -> dict:
    keys = jax.random.split(jax.random.key(seed), 5)
    return {
        "tile_sums": gaussian(keys[0], (RECORDS, NF, TCELLS), 30.0, 180.0, ((0, 128),)),
        "tile_dest": draw_tile_dest(jax.random.fold_in(keys[4], 71), 0),
        "tile_place": touch_ends(jax.random.randint(keys[2], (RECORDS,), 0, BX * BY), jax.random.fold_in(keys[2], 1), 0, (BX * BY) - 1).astype(jnp.int32),
        "tile_count": draw_tile_count(jax.random.fold_in(keys[4], 71), 0),
    }


def gauss_taps():
    spread = RADIUS * 5.0 / 16.0
    raw_taps = [math.exp(-(offset * offset) / (2.0 * spread * spread)) for offset in range(-RADIUS, RADIUS + 1)]
    total_weight = sum(raw_taps)
    return [value / total_weight for value in raw_taps]


def smooth_axis(field, axis, taps):
    length = field.shape[axis]
    widths = [(0, 0)] * field.ndim
    widths[axis] = (RADIUS, RADIUS)
    padded = jnp.pad(field, widths)
    result = jnp.zeros_like(field)
    for offset, weight in enumerate(taps):
        result = result + weight * lax.slice_in_dim(padded, offset, offset + length, axis=axis)
    return result


def reference(tile_sums, tile_dest, tile_place, tile_count):
    tiles_across = N_GX * BX
    tiles_down = N_GY * BY
    start_grid = jnp.zeros((tiles_down, tiles_across, NF, TCELLS), jnp.float32)
    per_device = tile_sums.reshape(DEVICES, SLOTS, NF, TCELLS)
    dest_table = tile_dest.reshape(DEVICES, SLOTS)
    place_table = tile_place.reshape(DEVICES, SLOTS)

    def add_device(grid, element):
        records, target, placed, counted = element
        is_live = jnp.arange(SLOTS, dtype=jnp.int32) < counted
        tile_rows = (target % N_GY) * BY + placed // BX
        tile_cols = (target // N_GY) * BX + placed % BX
        masked = jnp.where(is_live[:, None, None], records.astype(jnp.float32), jnp.float32(0.0))
        return grid.at[tile_rows, tile_cols].add(masked), None

    grid, unused = lax.scan(add_device, start_grid, (per_device, dest_table, place_table, tile_count))
    grid = grid.reshape(tiles_down, tiles_across, NF, NZ, TE, TE)
    deposited = grid.transpose(2, 3, 0, 4, 1, 5).reshape(NF, NZ, tiles_down * TE, tiles_across * TE)
    taps = gauss_taps()

    def smooth_field(field):
        along_x = smooth_axis(field, 2, taps)
        along_y = smooth_axis(along_x, 1, taps)
        return smooth_axis(along_y, 0, taps)

    return lax.map(smooth_field, deposited)
```

```python
import math

import jax
import jax.numpy as jnp
import numpy as np
from jax import lax
from jax.sharding import PartitionSpec as P

TE = 32
BX = 4
BY = 4
RADIUS = 4
HIGHEST = lax.Precision.HIGHEST


def gauss_taps():
    spread = RADIUS * 5.0 / 16.0
    raw_taps = [
        math.exp(-(offset * offset) / (2.0 * spread * spread))
        for offset in range(-RADIUS, RADIUS + 1)
    ]
    total_weight = sum(raw_taps)
    return [value / total_weight for value in raw_taps]


def band(length_in, length_out, shift):
    taps = gauss_taps()
    mat = np.zeros((length_in, length_out), np.float32)
    for j in range(length_out):
        for k in range(2 * RADIUS + 1):
            i = j + shift + k - RADIUS
            if 0 <= i < length_in:
                mat[i, j] = taps[k]
    return jnp.asarray(mat)


def halo(cells, axis, dim, width):
    count = lax.axis_size(axis)
    ends = count - 1
    head = lax.slice_in_dim(cells, 0, width, axis=dim)
    tail = lax.slice_in_dim(cells, cells.shape[dim] - width, cells.shape[dim], axis=dim)
    return jnp.concatenate(
        [
            lax.ppermute(tail, axis, [(i, (i + 1) % count) for i in range(ends)]),
            cells,
            lax.ppermute(head, axis, [((i + 1) % count, i) for i in range(ends)]),
        ],
        axis=dim,
    )


def local(tile_sums, tile_dest, tile_place, tile_count):
    slot_count, fields, cells = tile_sums.shape
    planes = cells // (TE * TE)
    across = lax.axis_size("gx")
    column_count = lax.axis_size("gy")
    peer_count = across * column_count
    is_live = jnp.arange(slot_count, dtype=jnp.int32) < tile_count[0]
    targets = jnp.arange(peer_count, dtype=jnp.int32)
    chosen = tile_dest[None, :] == targets[:, None]
    pick = chosen.astype(jnp.bfloat16)
    out_place = jnp.sum(jnp.where(chosen & is_live[None, :], tile_place[None, :] + 1, 0), axis=1) - 1
    in_place = lax.all_to_all(out_place[:, None], ("gx", "gy"), 0, 0, tiled=True).reshape(peer_count)
    local_ids = jnp.arange(BX * BY, dtype=jnp.int32)
    landing = (in_place[None, :] == local_ids[:, None]).astype(jnp.bfloat16)
    height = BY * TE
    width = BX * TE
    wz = band(planes, planes, 0)
    wx = band(width + 2 * RADIUS, width, RADIUS)
    wy = band(height + 2 * RADIUS, height, RADIUS)
    rows = cells // 128
    outs = []
    for f in range(fields):
        record = tile_sums[:, f, :]
        outgoing = jnp.dot(pick, record, preferred_element_type=jnp.float32).astype(jnp.bfloat16)
        outgoing = outgoing.reshape(peer_count, rows, 128)
        incoming = lax.all_to_all(outgoing, ("gx", "gy"), 0, 0, tiled=True)
        deposited = jnp.einsum("ts,src->trc", landing, incoming, preferred_element_type=jnp.float32)
        deposited = deposited.reshape(BY, BX, planes, TE, TE).transpose(2, 0, 3, 1, 4)
        deposited = deposited.reshape(planes, height, width)
        along_z = jnp.einsum("io,iyx->oyx", wz, deposited, precision=HIGHEST)
        padded = halo(along_z, "gx", 2, RADIUS)
        along_x = jnp.einsum("zyi,ix->zyx", padded, wx, precision=HIGHEST)
        padded = halo(along_x, "gy", 1, RADIUS)
        along_y = jnp.einsum("iy,zix->zyx", wy, padded, precision=HIGHEST)
        outs.append(lax.all_to_all(along_y, "gx", 0, 2, tiled=True))
    return jnp.stack(outs, axis=0)


def solution(mesh):
    return jax.shard_map(
        local,
        mesh=mesh,
        in_specs=(P(("gx", "gy"), None, None), P(("gx", "gy")), P(("gx", "gy")), P(("gx", "gy"))),
        out_specs=P(None, "gx", "gy", None),
        check_vma=False,
    )
```

```python
import math

import jax
import jax.numpy as jnp
import numpy as np
from jax import lax
from jax.sharding import PartitionSpec as P

TE = 32
BX = 4
BY = 4
RADIUS = 4
HIGHEST = lax.Precision.HIGHEST


def gauss_taps():
    spread = RADIUS * 5.0 / 16.0
    raw_taps = [
        math.exp(-(offset * offset) / (2.0 * spread * spread))
        for offset in range(-RADIUS, RADIUS + 1)
    ]
    total_weight = sum(raw_taps)
    return [value / total_weight for value in raw_taps]


def band(length_in, length_out, shift):
    taps = gauss_taps()
    mat = np.zeros((length_in, length_out), np.float32)
    for j in range(length_out):
        for k in range(2 * RADIUS + 1):
            i = j + shift + k - RADIUS
            if 0 <= i < length_in:
                mat[i, j] = taps[k]
    return jnp.asarray(mat)


def halo(cells, axis, dim, width):
    count = lax.axis_size(axis)
    ends = count - 1
    head = lax.slice_in_dim(cells, 0, width, axis=dim)
    tail = lax.slice_in_dim(cells, cells.shape[dim] - width, cells.shape[dim], axis=dim)
    return jnp.concatenate(
        [
            lax.ppermute(tail, axis, [(i, (i + 1) % count) for i in range(ends)]),
            cells,
            lax.ppermute(head, axis, [((i + 1) % count, i) for i in range(ends)]),
        ],
        axis=dim,
    )


def local(tile_sums, tile_dest, tile_place, tile_count):
    slot_count, fields, cells = tile_sums.shape
    planes = cells // (TE * TE)
    across = lax.axis_size("gx")
    column_count = lax.axis_size("gy")
    peer_count = across * column_count
    is_live = jnp.arange(slot_count, dtype=jnp.int32) < tile_count[0]
    targets = jnp.arange(peer_count, dtype=jnp.int32)
    chosen = tile_dest[None, :] == targets[:, None]
    pick = chosen.astype(jnp.bfloat16)
    out_place = jnp.sum(jnp.where(chosen & is_live[None, :], tile_place[None, :] + 1, 0), axis=1) - 1
    in_place = lax.all_to_all(out_place[:, None], ("gx", "gy"), 0, 0, tiled=True).reshape(peer_count)
    local_ids = jnp.arange(BX * BY, dtype=jnp.int32)
    landing = (in_place[None, :] == local_ids[:, None]).astype(jnp.bfloat16)
    height = BY * TE
    width = BX * TE
    wz = band(planes, planes, 0)
    wx = band(width + 2 * RADIUS, width, RADIUS)
    wy = band(height + 2 * RADIUS, height, RADIUS)
    rows = cells // 128

    def send(f):
        record = tile_sums[:, f, :]
        outgoing = jnp.dot(pick, record, preferred_element_type=jnp.float32).astype(jnp.bfloat16)
        outgoing = outgoing.reshape(peer_count, rows, 128)
        return lax.all_to_all(outgoing, ("gx", "gy"), 0, 0, tiled=True)

    def proc(incoming):
        deposited = jnp.einsum("ts,src->trc", landing, incoming, preferred_element_type=jnp.float32)
        deposited = deposited.reshape(BY, BX, planes, TE, TE).transpose(2, 0, 3, 1, 4)
        deposited = deposited.reshape(planes, height, width)
        along_z = jnp.einsum("io,iyx->oyx", wz, deposited, precision=HIGHEST)
        padded = halo(along_z, "gx", 2, RADIUS)
        along_x = jnp.einsum("zyi,ix->zyx", padded, wx, precision=HIGHEST)
        padded = halo(along_x, "gy", 1, RADIUS)
        along_y = jnp.einsum("iy,zix->zyx", wy, padded, precision=HIGHEST)
        return lax.all_to_all(along_y, "gx", 0, 2, tiled=True)

    outs = []
    incoming = send(0)
    for f in range(fields):
        if f + 1 < fields:
            following = send(f + 1)
            outs.append(proc(incoming))
            incoming = following
        else:
            outs.append(proc(incoming))
    return jnp.stack(outs, axis=0)


def solution(mesh):
    return jax.shard_map(
        local,
        mesh=mesh,
        in_specs=(P(("gx", "gy"), None, None), P(("gx", "gy")), P(("gx", "gy")), P(("gx", "gy"))),
        out_specs=P(None, "gx", "gy", None),
        check_vma=False,
    )
```

```python
import math

import jax
import jax.numpy as jnp
import numpy as np
from jax import lax
from jax.sharding import PartitionSpec as P

TE = 32
BX = 4
BY = 4
RADIUS = 4
HIGHEST = lax.Precision.HIGHEST


def gauss_taps():
    spread = RADIUS * 5.0 / 16.0
    raw_taps = [
        math.exp(-(offset * offset) / (2.0 * spread * spread))
        for offset in range(-RADIUS, RADIUS + 1)
    ]
    total_weight = sum(raw_taps)
    return [value / total_weight for value in raw_taps]


def band(length_in, length_out, shift):
    taps = gauss_taps()
    mat = np.zeros((length_in, length_out), np.float32)
    for j in range(length_out):
        for k in range(2 * RADIUS + 1):
            i = j + shift + k - RADIUS
            if 0 <= i < length_in:
                mat[i, j] = taps[k]
    return jnp.asarray(mat)


def halo(cells, axis, dim, width):
    count = lax.axis_size(axis)
    ends = count - 1
    head = lax.slice_in_dim(cells, 0, width, axis=dim)
    tail = lax.slice_in_dim(cells, cells.shape[dim] - width, cells.shape[dim], axis=dim)
    return jnp.concatenate(
        [
            lax.ppermute(tail, axis, [(i, (i + 1) % count) for i in range(ends)]),
            cells,
            lax.ppermute(head, axis, [((i + 1) % count, i) for i in range(ends)]),
        ],
        axis=dim,
    )


def local(tile_sums, tile_dest, tile_place, tile_count):
    slot_count, fields, cells = tile_sums.shape
    planes = cells // (TE * TE)
    across = lax.axis_size("gx")
    column_count = lax.axis_size("gy")
    peer_count = across * column_count
    targets = jnp.arange(peer_count, dtype=jnp.int32)
    pick = (tile_dest[None, :] == targets[:, None]).astype(jnp.bfloat16)
    table = jnp.stack([tile_dest, tile_place, jnp.broadcast_to(tile_count, (slot_count,))])
    every = lax.all_gather(table, ("gx", "gy"))
    every_dest, every_place, every_count = every[:, 0], every[:, 1], every[:, 2, 0]
    me = lax.axis_index("gx") * column_count + lax.axis_index("gy")
    slots = jnp.arange(slot_count, dtype=jnp.int32)
    mine = (every_dest == me) & (slots[None, :] < every_count[:, None])
    in_place = jnp.sum(jnp.where(mine, every_place + 1, 0), axis=1) - 1
    local_ids = jnp.arange(BX * BY, dtype=jnp.int32)
    landing = (in_place[None, :] == local_ids[:, None]).astype(jnp.bfloat16)
    height = BY * TE
    width = BX * TE
    wz = band(planes, planes, 0)
    wy = band(height + 2 * RADIUS, height, RADIUS)
    rows = cells // 128

    def send(f):
        record = tile_sums[:, f, :]
        outgoing = jnp.dot(pick, record, preferred_element_type=jnp.float32).astype(jnp.bfloat16)
        outgoing = outgoing.reshape(peer_count, rows, 128)
        return lax.all_to_all(outgoing, ("gx", "gy"), 0, 0, tiled=True)

    def proc(incoming):
        deposited = jnp.einsum("ts,src->trc", landing, incoming, preferred_element_type=jnp.float32)
        deposited = deposited.reshape(BY, BX, planes, TE, TE).transpose(2, 0, 3, 1, 4)
        deposited = deposited.reshape(planes, height, width)
        along_z = jnp.einsum("io,iyx->oyx", wz, deposited, precision=HIGHEST)
        padded = halo(along_z, "gy", 1, RADIUS)
        return jnp.einsum("iy,zix->zyx", wy, padded, precision=HIGHEST)

    def gather_x(along_y):
        return lax.all_to_all(along_y, "gx", 1, 3, tiled=True)

    def along_x(slab):
        count = slab.shape[0]
        blocks = slab.reshape(count * height, across, width)
        edge = jnp.zeros((count * height, 1, width), blocks.dtype)
        padded = jnp.concatenate([edge, blocks, edge], axis=1)
        result = jnp.einsum("rjx,xo->rjo", padded[:, 1 : across + 1], w_mid, precision=HIGHEST)
        result = result + jnp.einsum("rjx,xo->rjo", padded[:, 0:across], w_left, precision=HIGHEST)
        result = result + jnp.einsum("rjx,xo->rjo", padded[:, 2 : across + 2], w_right, precision=HIGHEST)
        return result.reshape(slab.shape)

    w_mid = band(width, width, 0)
    w_left = band(width, width, width)
    w_right = band(width, width, -width)
    smoothed = []
    incoming = send(0)
    for f in range(fields - 1):
        following = send(f + 1)
        smoothed.append(proc(incoming))
        incoming = following
    first = gather_x(jnp.stack(smoothed, axis=0))
    last = proc(incoming)
    last = gather_x(last[None])
    first = along_x(first)
    result = jnp.zeros((fields,) + first.shape[1:], first.dtype)
    result = lax.dynamic_update_slice_in_dim(result, first, 0, axis=0)
    return lax.dynamic_update_slice_in_dim(result, along_x(last), fields - 1, axis=0)


def solution(mesh):
    return jax.shard_map(
        local,
        mesh=mesh,
        in_specs=(P(("gx", "gy"), None, None), P(("gx", "gy")), P(("gx", "gy")), P(("gx", "gy"))),
        out_specs=P(None, "gx", "gy", None),
        check_vma=False,
    )
```

```python
import math

import jax
import jax.numpy as jnp
import numpy as np
from jax import lax
from jax.sharding import PartitionSpec as P

TE = 32
BX = 4
BY = 4
RADIUS = 4
HIGHEST = lax.Precision.HIGHEST


def gauss_taps():
    spread = RADIUS * 5.0 / 16.0
    raw_taps = [
        math.exp(-(offset * offset) / (2.0 * spread * spread))
        for offset in range(-RADIUS, RADIUS + 1)
    ]
    total_weight = sum(raw_taps)
    return [value / total_weight for value in raw_taps]


def band(length_in, length_out, shift):
    taps = gauss_taps()
    mat = np.zeros((length_in, length_out), np.float32)
    for j in range(length_out):
        for k in range(2 * RADIUS + 1):
            i = j + shift + k - RADIUS
            if 0 <= i < length_in:
                mat[i, j] = taps[k]
    return jnp.asarray(mat)


def halo(cells, axis, dim, width):
    count = lax.axis_size(axis)
    ends = count - 1
    head = lax.slice_in_dim(cells, 0, width, axis=dim)
    tail = lax.slice_in_dim(cells, cells.shape[dim] - width, cells.shape[dim], axis=dim)
    return jnp.concatenate(
        [
            lax.ppermute(tail, axis, [(i, (i + 1) % count) for i in range(ends)]),
            cells,
            lax.ppermute(head, axis, [((i + 1) % count, i) for i in range(ends)]),
        ],
        axis=dim,
    )


def local(tile_sums, tile_dest, tile_place, tile_count):
    slot_count, fields, cells = tile_sums.shape
    planes = cells // (TE * TE)
    across = lax.axis_size("gx")
    column_count = lax.axis_size("gy")
    peer_count = across * column_count
    is_live = jnp.arange(slot_count, dtype=jnp.int32) < tile_count[0]
    targets = jnp.arange(peer_count, dtype=jnp.int32)
    chosen = tile_dest[None, :] == targets[:, None]
    pick = chosen.astype(jnp.bfloat16)
    out_place = jnp.sum(jnp.where(chosen & is_live[None, :], tile_place[None, :] + 1, 0), axis=1) - 1
    rows = cells // 128

    def send(f):
        record = tile_sums[:, f, :]
        outgoing = jnp.dot(pick, record, preferred_element_type=jnp.float32).astype(jnp.bfloat16)
        outgoing = outgoing.reshape(peer_count, rows, 128)
        return lax.all_to_all(outgoing, ("gx", "gy"), 0, 0, tiled=True)

    incoming = send(0)
    in_place = lax.all_to_all(out_place[:, None], ("gx", "gy"), 0, 0, tiled=True).reshape(peer_count)
    local_ids = jnp.arange(BX * BY, dtype=jnp.int32)
    landing = (in_place[None, :] == local_ids[:, None]).astype(jnp.bfloat16)
    height = BY * TE
    width = BX * TE
    wz = band(planes, planes, 0)
    wy = band(height + 2 * RADIUS, height, RADIUS)
    rows = cells // 128

    def proc(incoming):
        deposited = jnp.einsum("ts,src->trc", landing, incoming, preferred_element_type=jnp.float32)
        deposited = deposited.reshape(BY, BX, planes, TE, TE).transpose(2, 0, 3, 1, 4)
        deposited = deposited.reshape(planes, height, width)
        along_z = jnp.einsum("io,iyx->oyx", wz, deposited, precision=HIGHEST)
        padded = halo(along_z, "gy", 1, RADIUS)
        return jnp.einsum("iy,zix->zyx", wy, padded, precision=HIGHEST)

    def gather_x(along_y):
        return lax.all_to_all(along_y, "gx", 1, 3, tiled=True)

    def along_x(slab):
        count = slab.shape[0]
        blocks = slab.reshape(count * height, across, width)
        edge = jnp.zeros((count * height, 1, width), blocks.dtype)
        padded = jnp.concatenate([edge, blocks, edge], axis=1)
        result = jnp.einsum("rjx,xo->rjo", padded[:, 1 : across + 1], w_mid, precision=HIGHEST)
        result = result + jnp.einsum("rjx,xo->rjo", padded[:, 0:across], w_left, precision=HIGHEST)
        result = result + jnp.einsum("rjx,xo->rjo", padded[:, 2 : across + 2], w_right, precision=HIGHEST)
        return result.reshape(slab.shape)

    w_mid = band(width, width, 0)
    w_left = band(width, width, width)
    w_right = band(width, width, -width)
    smoothed = []
    for f in range(fields - 1):
        following = send(f + 1)
        smoothed.append(proc(incoming))
        incoming = following
    first = gather_x(jnp.stack(smoothed, axis=0))
    last = proc(incoming)
    last = gather_x(last[None])
    first = along_x(first)
    last = along_x(last)
    return jnp.concatenate([first, last], axis=0)


def solution(mesh):
    return jax.shard_map(
        local,
        mesh=mesh,
        in_specs=(P(("gx", "gy"), None, None), P(("gx", "gy")), P(("gx", "gy")), P(("gx", "gy"))),
        out_specs=P(None, "gx", "gy", None),
        check_vma=False,
    )
```

```python
import math

import jax
import jax.numpy as jnp
import numpy as np
from jax import lax
from jax.sharding import PartitionSpec as P

TE = 32
BX = 4
BY = 4
RADIUS = 4
HIGHEST = lax.Precision.HIGHEST


def gauss_taps():
    spread = RADIUS * 5.0 / 16.0
    raw_taps = [
        math.exp(-(offset * offset) / (2.0 * spread * spread))
        for offset in range(-RADIUS, RADIUS + 1)
    ]
    total_weight = sum(raw_taps)
    return [value / total_weight for value in raw_taps]


def band(length_in, length_out, shift):
    taps = gauss_taps()
    mat = np.zeros((length_in, length_out), np.float32)
    for j in range(length_out):
        for k in range(2 * RADIUS + 1):
            i = j + shift + k - RADIUS
            if 0 <= i < length_in:
                mat[i, j] = taps[k]
    return jnp.asarray(mat)


def halo(cells, axis, dim, width):
    count = lax.axis_size(axis)
    ends = count - 1
    head = lax.slice_in_dim(cells, 0, width, axis=dim)
    tail = lax.slice_in_dim(cells, cells.shape[dim] - width, cells.shape[dim], axis=dim)
    return jnp.concatenate(
        [
            lax.ppermute(tail, axis, [(i, (i + 1) % count) for i in range(ends)]),
            cells,
            lax.ppermute(head, axis, [((i + 1) % count, i) for i in range(ends)]),
        ],
        axis=dim,
    )


def local(tile_sums, tile_dest, tile_place, tile_count):
    slot_count, fields, cells = tile_sums.shape
    planes = cells // (TE * TE)
    across = lax.axis_size("gx")
    column_count = lax.axis_size("gy")
    peer_count = across * column_count
    is_live = jnp.arange(slot_count, dtype=jnp.int32) < tile_count[0]
    targets = jnp.arange(peer_count, dtype=jnp.int32)
    chosen = tile_dest[None, :] == targets[:, None]
    pick = chosen.astype(jnp.bfloat16)
    out_place = jnp.sum(jnp.where(chosen & is_live[None, :], tile_place[None, :] + 1, 0), axis=1) - 1

    def send(f):
        record = tile_sums[:, f, :]
        outgoing = jnp.dot(pick, record, preferred_element_type=jnp.float32).astype(jnp.bfloat16)
        outgoing = outgoing.reshape(peer_count, rows, 128)
        if f == 0:
            marks = jnp.broadcast_to(out_place.astype(jnp.bfloat16)[:, None, None], (peer_count, 8, 128))
            outgoing = jnp.concatenate([outgoing, marks], axis=1)
        return lax.all_to_all(outgoing, ("gx", "gy"), 0, 0, tiled=True)

    rows = cells // 128
    incoming = send(0)
    in_place = incoming[:, rows, 0].astype(jnp.int32)
    incoming = incoming[:, :rows]
    local_ids = jnp.arange(BX * BY, dtype=jnp.int32)
    landing = (in_place[None, :] == local_ids[:, None]).astype(jnp.bfloat16)
    height = BY * TE
    width = BX * TE
    wz = band(planes, planes, 0)
    wy = band(height + 2 * RADIUS, height, RADIUS)
    rows = cells // 128

    def proc(incoming):
        deposited = jnp.einsum("ts,src->trc", landing, incoming, preferred_element_type=jnp.float32)
        deposited = deposited.reshape(BY, BX, planes, TE, TE).transpose(2, 0, 3, 1, 4)
        deposited = deposited.reshape(planes, height, width)
        along_z = jnp.einsum("io,iyx->oyx", wz, deposited, precision=HIGHEST)
        padded = halo(along_z, "gy", 1, RADIUS)
        return jnp.einsum("iy,zix->zyx", wy, padded, precision=HIGHEST)

    def gather_x(along_y):
        return lax.all_to_all(along_y, "gx", 1, 3, tiled=True)

    def along_x(slab):
        count = slab.shape[0]
        blocks = slab.reshape(count * height, across, width)
        edge = jnp.zeros((count * height, 1, width), blocks.dtype)
        padded = jnp.concatenate([edge, blocks, edge], axis=1)
        result = jnp.einsum("rjx,xo->rjo", padded[:, 1 : across + 1], w_mid, precision=HIGHEST)
        result = result + jnp.einsum("rjx,xo->rjo", padded[:, 0:across], w_left, precision=HIGHEST)
        result = result + jnp.einsum("rjx,xo->rjo", padded[:, 2 : across + 2], w_right, precision=HIGHEST)
        return result.reshape(slab.shape)

    w_mid = band(width, width, 0)
    w_left = band(width, width, width)
    w_right = band(width, width, -width)
    smoothed = []
    for f in range(fields - 1):
        following = send(f + 1)
        smoothed.append(proc(incoming))
        incoming = following
    first = gather_x(jnp.stack(smoothed, axis=0))
    last = proc(incoming)
    last = gather_x(last[None])
    first = along_x(first)
    last = along_x(last)
    return jnp.concatenate([first, last], axis=0)


def solution(mesh):
    return jax.shard_map(
        local,
        mesh=mesh,
        in_specs=(P(("gx", "gy"), None, None), P(("gx", "gy")), P(("gx", "gy")), P(("gx", "gy"))),
        out_specs=P(None, "gx", "gy", None),
        check_vma=False,
    )
```

```python
import math

import jax
import jax.numpy as jnp
import numpy as np
from jax import lax
from jax.sharding import PartitionSpec as P

TE = 32
BX = 4
BY = 4
RADIUS = 4
HIGHEST = lax.Precision.HIGHEST


def gauss_taps():
    spread = RADIUS * 5.0 / 16.0
    raw_taps = [
        math.exp(-(offset * offset) / (2.0 * spread * spread))
        for offset in range(-RADIUS, RADIUS + 1)
    ]
    total_weight = sum(raw_taps)
    return [value / total_weight for value in raw_taps]


def band(length_in, length_out, shift):
    taps = gauss_taps()
    mat = np.zeros((length_in, length_out), np.float32)
    for j in range(length_out):
        for k in range(2 * RADIUS + 1):
            i = j + shift + k - RADIUS
            if 0 <= i < length_in:
                mat[i, j] = taps[k]
    return jnp.asarray(mat)


def halo(cells, axis, dim, width):
    count = lax.axis_size(axis)
    ends = count - 1
    head = lax.slice_in_dim(cells, 0, width, axis=dim)
    tail = lax.slice_in_dim(cells, cells.shape[dim] - width, cells.shape[dim], axis=dim)
    return jnp.concatenate(
        [
            lax.ppermute(tail, axis, [(i, (i + 1) % count) for i in range(ends)]),
            cells,
            lax.ppermute(head, axis, [((i + 1) % count, i) for i in range(ends)]),
        ],
        axis=dim,
    )


def local(tile_sums, tile_dest, tile_place, tile_count):
    slot_count, fields, cells = tile_sums.shape
    planes = cells // (TE * TE)
    across = lax.axis_size("gx")
    column_count = lax.axis_size("gy")
    peer_count = across * column_count
    is_live = jnp.arange(slot_count, dtype=jnp.int32) < tile_count[0]
    targets = jnp.arange(peer_count, dtype=jnp.int32)
    chosen = tile_dest[None, :] == targets[:, None]
    pick = chosen.astype(jnp.bfloat16)
    out_place = jnp.sum(jnp.where(chosen & is_live[None, :], tile_place[None, :] + 1, 0), axis=1) - 1

    def send(f):
        record = tile_sums[:, f, :]
        outgoing = jnp.dot(pick, record, preferred_element_type=jnp.float32).astype(jnp.bfloat16)
        outgoing = outgoing.reshape(peer_count, rows, 128)
        if f == 0:
            marks = jnp.broadcast_to(out_place.astype(jnp.bfloat16)[:, None, None], (peer_count, 8, 128))
            outgoing = jnp.concatenate([outgoing, marks], axis=1)
        return lax.all_to_all(outgoing, ("gx", "gy"), 0, 0, tiled=True)

    rows = cells // 128
    incoming = send(0)
    in_place = incoming[:, rows, 0].astype(jnp.int32)
    incoming = incoming[:, :rows]
    local_ids = jnp.arange(BX * BY, dtype=jnp.int32)
    landing = (in_place[None, :] == local_ids[:, None]).astype(jnp.bfloat16)
    height = BY * TE
    width = BX * TE
    wz = band(planes, planes, 0)
    wy = band(height + 2 * RADIUS, height, RADIUS)
    rows = cells // 128

    def proc(incoming):
        deposited = jnp.einsum("ts,src->trc", landing, incoming, preferred_element_type=jnp.float32)
        deposited = deposited.reshape(BY, BX, planes, TE, TE).transpose(2, 0, 3, 1, 4)
        deposited = deposited.reshape(planes, height, width)
        along_z = jnp.einsum("io,iyx->oyx", wz, deposited, precision=HIGHEST)
        padded = halo(along_z, "gy", 1, RADIUS)
        return jnp.einsum("iy,zix->zyx", wy, padded, precision=HIGHEST)

    def gather_x(along_y):
        return lax.all_to_all(along_y, "gx", 1, 1, tiled=True)

    def along_x(blocks):
        count = blocks.shape[0]
        edge = jnp.zeros((count, 1, height, width), blocks.dtype)
        padded = jnp.concatenate([edge, blocks, edge], axis=1)
        result = jnp.einsum("fjyx,xo->fyjo", padded[:, 1 : across + 1], w_mid, precision=HIGHEST)
        result = result + jnp.einsum("fjyx,xo->fyjo", padded[:, 0:across], w_left, precision=HIGHEST)
        result = result + jnp.einsum("fjyx,xo->fyjo", padded[:, 2 : across + 2], w_right, precision=HIGHEST)
        return result.reshape(count, 1, height, across * width)

    w_mid = band(width, width, 0)
    w_left = band(width, width, width)
    w_right = band(width, width, -width)
    smoothed = []
    for f in range(fields - 1):
        following = send(f + 1)
        smoothed.append(proc(incoming))
        incoming = following
    first = gather_x(jnp.stack(smoothed, axis=0))
    last = proc(incoming)
    last = gather_x(last[None])
    spare = jnp.zeros((1,) + first.shape[1:], first.dtype)
    result = along_x(jnp.concatenate([first, spare], axis=0))
    return lax.dynamic_update_slice_in_dim(result, along_x(last), fields - 1, axis=0)


def solution(mesh):
    return jax.shard_map(
        local,
        mesh=mesh,
        in_specs=(P(("gx", "gy"), None, None), P(("gx", "gy")), P(("gx", "gy")), P(("gx", "gy"))),
        out_specs=P(None, "gx", "gy", None),
        check_vma=False,
    )
```

```python
import math

import jax
import jax.numpy as jnp
import numpy as np
from jax import lax
from jax.sharding import PartitionSpec as P

TE = 32
BX = 4
BY = 4
RADIUS = 4
HIGHEST = lax.Precision.HIGHEST


def gauss_taps():
    spread = RADIUS * 5.0 / 16.0
    raw_taps = [
        math.exp(-(offset * offset) / (2.0 * spread * spread))
        for offset in range(-RADIUS, RADIUS + 1)
    ]
    total_weight = sum(raw_taps)
    return [value / total_weight for value in raw_taps]


def band(length_in, length_out, shift):
    taps = gauss_taps()
    mat = np.zeros((length_in, length_out), np.float32)
    for j in range(length_out):
        for k in range(2 * RADIUS + 1):
            i = j + shift + k - RADIUS
            if 0 <= i < length_in:
                mat[i, j] = taps[k]
    return jnp.asarray(mat)


def halo(cells, axis, dim, width):
    count = lax.axis_size(axis)
    ends = count - 1
    head = lax.slice_in_dim(cells, 0, width, axis=dim)
    tail = lax.slice_in_dim(cells, cells.shape[dim] - width, cells.shape[dim], axis=dim)
    return jnp.concatenate(
        [
            lax.ppermute(tail, axis, [(i, (i + 1) % count) for i in range(ends)]),
            cells,
            lax.ppermute(head, axis, [((i + 1) % count, i) for i in range(ends)]),
        ],
        axis=dim,
    )


def local(tile_sums, tile_dest, tile_place, tile_count):
    slot_count, fields, cells = tile_sums.shape
    planes = cells // (TE * TE)
    across = lax.axis_size("gx")
    column_count = lax.axis_size("gy")
    peer_count = across * column_count
    is_live = jnp.arange(slot_count, dtype=jnp.int32) < tile_count[0]
    targets = jnp.arange(peer_count, dtype=jnp.int32)
    chosen = tile_dest[None, :] == targets[:, None]
    pick = chosen.astype(jnp.bfloat16)
    out_place = jnp.sum(jnp.where(chosen & is_live[None, :], tile_place[None, :] + 1, 0), axis=1) - 1

    def send(f):
        record = tile_sums[:, f, :]
        outgoing = jnp.dot(pick, record, preferred_element_type=jnp.float32).astype(jnp.bfloat16)
        outgoing = outgoing.reshape(peer_count, rows, 128)
        if f == 0:
            marks = jnp.broadcast_to(out_place.astype(jnp.bfloat16)[:, None, None], (peer_count, 8, 128))
            outgoing = jnp.concatenate([outgoing, marks], axis=1)
        return lax.all_to_all(outgoing, ("gx", "gy"), 0, 0, tiled=True)

    rows = cells // 128
    incoming = send(0)
    in_place = incoming[:, rows, 0].astype(jnp.int32)
    incoming = incoming[:, :rows]
    local_ids = jnp.arange(BX * BY, dtype=jnp.int32)
    landing = (in_place[None, :] == local_ids[:, None]).astype(jnp.bfloat16)
    height = BY * TE
    width = BX * TE
    wz = band(planes, planes, 0)
    wy = band(height + 2 * RADIUS, height, RADIUS)
    rows = cells // 128

    def proc(incoming):
        deposited = jnp.einsum("ts,src->trc", landing, incoming, preferred_element_type=jnp.float32)
        deposited = deposited.reshape(BY, BX, planes, TE, TE).transpose(2, 0, 3, 1, 4)
        deposited = deposited.reshape(planes, height, width)
        along_z = jnp.einsum("io,iyx->oyx", wz, deposited, precision=HIGHEST)
        padded = halo(along_z, "gy", 1, RADIUS)
        return jnp.einsum("iy,zix->zyx", wy, padded, precision=HIGHEST)

    def gather_x(along_y):
        return lax.all_to_all(along_y, "gx", 1, 1, tiled=True)

    def spread_x(along_y):
        me_x = lax.axis_index("gx")
        pieces = [lax.dynamic_slice_in_dim(along_y, me_x, 1, axis=0)]
        for shift in range(1, across):
            piece = lax.dynamic_slice_in_dim(along_y, (me_x + shift) % across, 1, axis=0)
            pieces.append(lax.ppermute(piece, "gx", [(g, (g + shift) % across) for g in range(across)]))
        stacked = jnp.concatenate(pieces, axis=0)
        order = (me_x - jnp.arange(across, dtype=jnp.int32)) % across
        return jnp.take(stacked, order, axis=0)[None]

    def along_x(blocks):
        count = blocks.shape[0]
        edge = jnp.zeros((count, 1, height, width), blocks.dtype)
        padded = jnp.concatenate([edge, blocks, edge], axis=1)
        result = jnp.einsum("fjyx,xo->fyjo", padded[:, 1 : across + 1], w_mid, precision=HIGHEST)
        result = result + jnp.einsum("fjyx,xo->fyjo", padded[:, 0:across], w_left, precision=HIGHEST)
        result = result + jnp.einsum("fjyx,xo->fyjo", padded[:, 2 : across + 2], w_right, precision=HIGHEST)
        return result.reshape(count, 1, height, across * width)

    w_mid = band(width, width, 0)
    w_left = band(width, width, width)
    w_right = band(width, width, -width)
    smoothed = []
    for f in range(fields - 1):
        following = send(f + 1)
        smoothed.append(proc(incoming))
        incoming = following
    first = gather_x(jnp.stack(smoothed, axis=0))
    last = proc(incoming)
    last = spread_x(last)
    spare = jnp.zeros((1,) + first.shape[1:], first.dtype)
    result = along_x(jnp.concatenate([first, spare], axis=0))
    return lax.dynamic_update_slice_in_dim(result, along_x(last), fields - 1, axis=0)


def solution(mesh):
    return jax.shard_map(
        local,
        mesh=mesh,
        in_specs=(P(("gx", "gy"), None, None), P(("gx", "gy")), P(("gx", "gy")), P(("gx", "gy"))),
        out_specs=P(None, "gx", "gy", None),
        check_vma=False,
    )
```

```python
import math

import jax
import jax.numpy as jnp
import numpy as np
from jax import lax
from jax.sharding import PartitionSpec as P

TE = 32
BX = 4
BY = 4
RADIUS = 4
HIGHEST = lax.Precision.HIGHEST
HIGH = lax.Precision.HIGH


def gauss_taps():
    spread = RADIUS * 5.0 / 16.0
    raw_taps = [
        math.exp(-(offset * offset) / (2.0 * spread * spread))
        for offset in range(-RADIUS, RADIUS + 1)
    ]
    total_weight = sum(raw_taps)
    return [value / total_weight for value in raw_taps]


def band(length_in, length_out, shift):
    taps = gauss_taps()
    mat = np.zeros((length_in, length_out), np.float32)
    for j in range(length_out):
        for k in range(2 * RADIUS + 1):
            i = j + shift + k - RADIUS
            if 0 <= i < length_in:
                mat[i, j] = taps[k]
    return jnp.asarray(mat)


def halo(cells, axis, dim, width):
    count = lax.axis_size(axis)
    ends = count - 1
    head = lax.slice_in_dim(cells, 0, width, axis=dim)
    tail = lax.slice_in_dim(cells, cells.shape[dim] - width, cells.shape[dim], axis=dim)
    return jnp.concatenate(
        [
            lax.ppermute(tail, axis, [(i, (i + 1) % count) for i in range(ends)]),
            cells,
            lax.ppermute(head, axis, [((i + 1) % count, i) for i in range(ends)]),
        ],
        axis=dim,
    )


def local(tile_sums, tile_dest, tile_place, tile_count):
    slot_count, fields, cells = tile_sums.shape
    planes = cells // (TE * TE)
    across = lax.axis_size("gx")
    column_count = lax.axis_size("gy")
    peer_count = across * column_count
    is_live = jnp.arange(slot_count, dtype=jnp.int32) < tile_count[0]
    targets = jnp.arange(peer_count, dtype=jnp.int32)
    chosen = tile_dest[None, :] == targets[:, None]
    pick = chosen.astype(jnp.bfloat16)
    out_place = jnp.sum(jnp.where(chosen & is_live[None, :], tile_place[None, :] + 1, 0), axis=1) - 1

    def send(f):
        record = tile_sums[:, f, :]
        outgoing = jnp.dot(pick, record, preferred_element_type=jnp.float32).astype(jnp.bfloat16)
        outgoing = outgoing.reshape(peer_count, rows, 128)
        if f == 0:
            marks = jnp.broadcast_to(out_place.astype(jnp.bfloat16)[:, None, None], (peer_count, 8, 128))
            outgoing = jnp.concatenate([outgoing, marks], axis=1)
        return lax.all_to_all(outgoing, ("gx", "gy"), 0, 0, tiled=True)

    rows = cells // 128
    incoming = send(0)
    in_place = incoming[:, rows, 0].astype(jnp.int32)
    incoming = incoming[:, :rows]
    local_ids = jnp.arange(BX * BY, dtype=jnp.int32)
    landing = (in_place[None, :] == local_ids[:, None]).astype(jnp.bfloat16)
    height = BY * TE
    width = BX * TE
    wz = band(planes, planes, 0)
    wy = band(height + 2 * RADIUS, height, RADIUS)
    rows = cells // 128

    def proc(incoming):
        deposited = jnp.einsum("ts,src->trc", landing, incoming, preferred_element_type=jnp.float32)
        deposited = deposited.reshape(BY, BX, planes, TE, TE).transpose(2, 0, 3, 1, 4)
        deposited = deposited.reshape(planes, height, width)
        along_z = jnp.einsum("io,iyx->oyx", wz, deposited, precision=HIGHEST)
        padded = halo(along_z, "gy", 1, RADIUS)
        return jnp.einsum("iy,zix->zyx", wy, padded, precision=HIGHEST)

    def gather_x(along_y):
        return lax.all_to_all(along_y, "gx", 1, 1, tiled=True)

    def spread_x(along_y):
        me_x = lax.axis_index("gx")
        pieces = [lax.dynamic_slice_in_dim(along_y, me_x, 1, axis=0)]
        for shift in range(1, across):
            piece = lax.dynamic_slice_in_dim(along_y, (me_x + shift) % across, 1, axis=0)
            pieces.append(lax.ppermute(piece, "gx", [(g, (g + shift) % across) for g in range(across)]))
        stacked = jnp.concatenate(pieces, axis=0)
        order = (me_x - jnp.arange(across, dtype=jnp.int32)) % across
        return jnp.take(stacked, order, axis=0)[None]

    def along_x(blocks):
        count = blocks.shape[0]
        edge = jnp.zeros((count, 1, height, width), blocks.dtype)
        padded = jnp.concatenate([edge, blocks, edge], axis=1)
        result = jnp.einsum("fjyx,xo->fyjo", padded[:, 1 : across + 1], w_mid, precision=HIGH)
        result = result + jnp.einsum("fjyx,xo->fyjo", padded[:, 0:across], w_left, precision=HIGH)
        result = result + jnp.einsum("fjyx,xo->fyjo", padded[:, 2 : across + 2], w_right, precision=HIGH)
        return result.reshape(count, 1, height, across * width)

    w_mid = band(width, width, 0)
    w_left = band(width, width, width)
    w_right = band(width, width, -width)
    smoothed = []
    for f in range(fields - 1):
        following = send(f + 1)
        smoothed.append(proc(incoming))
        incoming = following
    first = gather_x(jnp.stack(smoothed, axis=0))
    last = proc(incoming)
    last = spread_x(last)
    spare = jnp.zeros((1,) + first.shape[1:], first.dtype)
    result = along_x(jnp.concatenate([first, spare], axis=0))
    return lax.dynamic_update_slice_in_dim(result, along_x(last), fields - 1, axis=0)


def solution(mesh):
    return jax.shard_map(
        local,
        mesh=mesh,
        in_specs=(P(("gx", "gy"), None, None), P(("gx", "gy")), P(("gx", "gy")), P(("gx", "gy"))),
        out_specs=P(None, "gx", "gy", None),
        check_vma=False,
    )
```

```python
import math

import jax
import jax.numpy as jnp
import numpy as np
from jax import lax
from jax.sharding import PartitionSpec as P

TE = 32
BX = 4
BY = 4
RADIUS = 4
HIGHEST = lax.Precision.HIGHEST
HIGH = lax.Precision.HIGH


def gauss_taps():
    spread = RADIUS * 5.0 / 16.0
    raw_taps = [
        math.exp(-(offset * offset) / (2.0 * spread * spread))
        for offset in range(-RADIUS, RADIUS + 1)
    ]
    total_weight = sum(raw_taps)
    return [value / total_weight for value in raw_taps]


def band(length_in, length_out, shift):
    taps = gauss_taps()
    mat = np.zeros((length_in, length_out), np.float32)
    for j in range(length_out):
        for k in range(2 * RADIUS + 1):
            i = j + shift + k - RADIUS
            if 0 <= i < length_in:
                mat[i, j] = taps[k]
    return jnp.asarray(mat)


def halo(cells, axis, dim, width):
    count = lax.axis_size(axis)
    ends = count - 1
    head = lax.slice_in_dim(cells, 0, width, axis=dim)
    tail = lax.slice_in_dim(cells, cells.shape[dim] - width, cells.shape[dim], axis=dim)
    return jnp.concatenate(
        [
            lax.ppermute(tail, axis, [(i, (i + 1) % count) for i in range(ends)]),
            cells,
            lax.ppermute(head, axis, [((i + 1) % count, i) for i in range(ends)]),
        ],
        axis=dim,
    )


def local(tile_sums, tile_dest, tile_place, tile_count):
    slot_count, fields, cells = tile_sums.shape
    planes = cells // (TE * TE)
    across = lax.axis_size("gx")
    column_count = lax.axis_size("gy")
    peer_count = across * column_count
    is_live = jnp.arange(slot_count, dtype=jnp.int32) < tile_count[0]
    targets = jnp.arange(peer_count, dtype=jnp.int32)
    chosen = tile_dest[None, :] == targets[:, None]
    pick = chosen.astype(jnp.bfloat16)
    out_place = jnp.sum(jnp.where(chosen & is_live[None, :], tile_place[None, :] + 1, 0), axis=1) - 1

    def send(f):
        record = tile_sums[:, f, :]
        outgoing = jnp.dot(pick, record, preferred_element_type=jnp.float32).astype(jnp.bfloat16)
        outgoing = outgoing.reshape(peer_count, rows, 128)
        if f == 0:
            marks = jnp.broadcast_to(out_place.astype(jnp.bfloat16)[:, None, None], (peer_count, 8, 128))
            outgoing = jnp.concatenate([outgoing, marks], axis=1)
        return lax.all_to_all(outgoing, ("gx", "gy"), 0, 0, tiled=True)

    rows = cells // 128
    incoming = send(0)
    in_place = incoming[:, rows, 0].astype(jnp.int32)
    incoming = incoming[:, :rows]
    local_ids = jnp.arange(BX * BY, dtype=jnp.int32)
    landing = (in_place[None, :] == local_ids[:, None]).astype(jnp.bfloat16)
    height = BY * TE
    width = BX * TE
    wz = band(planes, planes, 0)
    wy = band(height + 2 * RADIUS, height, RADIUS)
    rows = cells // 128

    def proc(incoming):
        deposited = jnp.einsum("ts,src->trc", landing, incoming, preferred_element_type=jnp.float32)
        deposited = deposited.reshape(BY, BX, planes, TE, TE).transpose(2, 0, 3, 1, 4)
        deposited = deposited.reshape(planes, height, width)
        along_z = jnp.einsum("io,iyx->oyx", wz, deposited, precision=HIGHEST)
        padded = halo(along_z, "gy", 1, RADIUS)
        return jnp.einsum("iy,zix->zxy", wy, padded, precision=HIGHEST)

    def gather_x(along_y):
        return lax.all_to_all(along_y, "gx", 1, 1, tiled=True)

    def spread_x(along_y):
        me_x = lax.axis_index("gx")
        pieces = [lax.dynamic_slice_in_dim(along_y, me_x, 1, axis=0)]
        for shift in range(1, across):
            piece = lax.dynamic_slice_in_dim(along_y, (me_x + shift) % across, 1, axis=0)
            pieces.append(lax.ppermute(piece, "gx", [(g, (g + shift) % across) for g in range(across)]))
        stacked = jnp.concatenate(pieces, axis=0)
        order = (me_x - jnp.arange(across, dtype=jnp.int32)) % across
        return jnp.take(stacked, order, axis=0)[None]

    def along_x(blocks):
        count = blocks.shape[0]
        edge = jnp.zeros((count, 1, width, height), blocks.dtype)
        padded = jnp.concatenate([edge, blocks, edge], axis=1)
        result = jnp.einsum("fjxy,xo->fyjo", padded[:, 1 : across + 1], w_mid, precision=HIGH)
        result = result + jnp.einsum("fjxy,xo->fyjo", padded[:, 0:across], w_left, precision=HIGH)
        result = result + jnp.einsum("fjxy,xo->fyjo", padded[:, 2 : across + 2], w_right, precision=HIGH)
        return result.reshape(count, 1, height, across * width)

    w_mid = band(width, width, 0)
    w_left = band(width, width, width)
    w_right = band(width, width, -width)
    smoothed = []
    for f in range(fields - 1):
        following = send(f + 1)
        smoothed.append(proc(incoming))
        incoming = following
    first = gather_x(jnp.stack(smoothed, axis=0))
    last = proc(incoming)
    last = spread_x(last)
    spare = jnp.zeros((1,) + first.shape[1:], first.dtype)
    result = along_x(jnp.concatenate([first, spare], axis=0))
    return lax.dynamic_update_slice_in_dim(result, along_x(last), fields - 1, axis=0)


def solution(mesh):
    return jax.shard_map(
        local,
        mesh=mesh,
        in_specs=(P(("gx", "gy"), None, None), P(("gx", "gy")), P(("gx", "gy")), P(("gx", "gy"))),
        out_specs=P(None, "gx", "gy", None),
        check_vma=False,
    )
```

```python
import math

import jax
import jax.numpy as jnp
import numpy as np
from jax import lax
from jax.sharding import PartitionSpec as P

TE = 32
BX = 4
BY = 4
RADIUS = 4
HIGHEST = lax.Precision.HIGHEST


def gauss_taps():
    spread = RADIUS * 5.0 / 16.0
    raw_taps = [
        math.exp(-(offset * offset) / (2.0 * spread * spread))
        for offset in range(-RADIUS, RADIUS + 1)
    ]
    total_weight = sum(raw_taps)
    return [value / total_weight for value in raw_taps]


def band(length_in, length_out, shift):
    taps = gauss_taps()
    mat = np.zeros((length_in, length_out), np.float32)
    for j in range(length_out):
        for k in range(2 * RADIUS + 1):
            i = j + shift + k - RADIUS
            if 0 <= i < length_in:
                mat[i, j] = taps[k]
    return jnp.asarray(mat)


def halo(cells, axis, dim, width):
    count = lax.axis_size(axis)
    ends = count - 1
    head = lax.slice_in_dim(cells, 0, width, axis=dim)
    tail = lax.slice_in_dim(cells, cells.shape[dim] - width, cells.shape[dim], axis=dim)
    return jnp.concatenate(
        [
            lax.ppermute(tail, axis, [(i, (i + 1) % count) for i in range(ends)]),
            cells,
            lax.ppermute(head, axis, [((i + 1) % count, i) for i in range(ends)]),
        ],
        axis=dim,
    )


def local(tile_sums, tile_dest, tile_place, tile_count):
    slot_count, fields, cells = tile_sums.shape
    planes = cells // (TE * TE)
    across = lax.axis_size("gx")
    column_count = lax.axis_size("gy")
    peer_count = across * column_count
    is_live = jnp.arange(slot_count, dtype=jnp.int32) < tile_count[0]
    targets = jnp.arange(peer_count, dtype=jnp.int32)
    chosen = tile_dest[None, :] == targets[:, None]
    pick = chosen.astype(jnp.bfloat16)
    out_place = jnp.sum(jnp.where(chosen & is_live[None, :], tile_place[None, :] + 1, 0), axis=1) - 1

    def send(f):
        record = tile_sums[:, f, :]
        outgoing = jnp.dot(pick, record, preferred_element_type=jnp.float32).astype(jnp.bfloat16)
        outgoing = outgoing.reshape(peer_count, rows, 128)
        if f == 0:
            marks = jnp.broadcast_to(out_place.astype(jnp.bfloat16)[:, None, None], (peer_count, 8, 128))
            outgoing = jnp.concatenate([outgoing, marks], axis=1)
        return lax.all_to_all(outgoing, ("gx", "gy"), 0, 0, tiled=True)

    rows = cells // 128
    incoming = send(0)
    in_place = incoming[:, rows, 0].astype(jnp.int32)
    incoming = incoming[:, :rows]
    local_ids = jnp.arange(BX * BY, dtype=jnp.int32)
    landing = (in_place[None, :] == local_ids[:, None]).astype(jnp.bfloat16)
    height = BY * TE
    width = BX * TE
    wz = band(planes, planes, 0)
    wy = band(height + 2 * RADIUS, height, RADIUS)
    rows = cells // 128

    def proc(incoming):
        deposited = jnp.einsum("ts,src->trc", landing, incoming, preferred_element_type=jnp.float32)
        deposited = deposited.reshape(BY, BX, planes, TE, TE).transpose(2, 0, 3, 1, 4)
        deposited = deposited.reshape(planes, height, width)
        along_z = jnp.einsum("io,iyx->oyx", wz, deposited, precision=HIGHEST)
        padded = halo(along_z, "gy", 1, RADIUS)
        return jnp.einsum("iy,zix->zxy", wy, padded, precision=HIGHEST)

    def gather_x(along_y):
        return lax.all_to_all(along_y, "gx", 1, 1, tiled=True)

    def spread_x(along_y):
        me_x = lax.axis_index("gx")
        pieces = [lax.dynamic_slice_in_dim(along_y, me_x, 1, axis=0)]
        for shift in range(1, across):
            piece = lax.dynamic_slice_in_dim(along_y, (me_x + shift) % across, 1, axis=0)
            pieces.append(lax.ppermute(piece, "gx", [(g, (g + shift) % across) for g in range(across)]))
        stacked = jnp.concatenate(pieces, axis=0)
        order = (me_x - jnp.arange(across, dtype=jnp.int32)) % across
        return jnp.take(stacked, order, axis=0)[None]

    def along_x(blocks):
        count = blocks.shape[0]
        edge = jnp.zeros((count, 1, width, height), blocks.dtype)
        padded = jnp.concatenate([edge, blocks, edge], axis=1)
        result = jnp.einsum("fjxy,xo->fyjo", padded[:, 1 : across + 1], w_mid, precision=HIGHEST)
        reach = width - RADIUS
        from_left = jnp.einsum("fjxy,xo->fyjo", padded[:, 0:across, reach:], w_left[reach:, :RADIUS], precision=HIGHEST)
        from_right = jnp.einsum(
            "fjxy,xo->fyjo", padded[:, 2 : across + 2, :RADIUS], w_right[:RADIUS, reach:], precision=HIGHEST
        )
        zeros = jnp.zeros(from_left.shape[:3] + (reach,), result.dtype)
        result = result + jnp.concatenate([from_left, zeros], axis=3) + jnp.concatenate([zeros, from_right], axis=3)
        return result.reshape(count, 1, height, across * width)

    w_mid = band(width, width, 0)
    w_left = band(width, width, width)
    w_right = band(width, width, -width)
    smoothed = []
    for f in range(fields - 1):
        following = send(f + 1)
        smoothed.append(proc(incoming))
        incoming = following
    first = gather_x(jnp.stack(smoothed, axis=0))
    last = proc(incoming)
    last = spread_x(last)
    spare = jnp.zeros((1,) + first.shape[1:], first.dtype)
    result = along_x(jnp.concatenate([first, spare], axis=0))
    return lax.dynamic_update_slice_in_dim(result, along_x(last), fields - 1, axis=0)


def solution(mesh):
    return jax.shard_map(
        local,
        mesh=mesh,
        in_specs=(P(("gx", "gy"), None, None), P(("gx", "gy")), P(("gx", "gy")), P(("gx", "gy"))),
        out_specs=P(None, "gx", "gy", None),
        check_vma=False,
    )
```

```python
import math

import jax
import jax.numpy as jnp
import numpy as np
from jax import lax
from jax.sharding import PartitionSpec as P

TE = 32
BX = 4
BY = 4
RADIUS = 4
HIGHEST = lax.Precision.HIGHEST


def gauss_taps():
    spread = RADIUS * 5.0 / 16.0
    raw_taps = [
        math.exp(-(offset * offset) / (2.0 * spread * spread))
        for offset in range(-RADIUS, RADIUS + 1)
    ]
    total_weight = sum(raw_taps)
    return [value / total_weight for value in raw_taps]


def band(length_in, length_out, shift):
    taps = gauss_taps()
    mat = np.zeros((length_in, length_out), np.float32)
    for j in range(length_out):
        for k in range(2 * RADIUS + 1):
            i = j + shift + k - RADIUS
            if 0 <= i < length_in:
                mat[i, j] = taps[k]
    return jnp.asarray(mat)


def halo(cells, axis, dim, width):
    count = lax.axis_size(axis)
    ends = count - 1
    head = lax.slice_in_dim(cells, 0, width, axis=dim)
    tail = lax.slice_in_dim(cells, cells.shape[dim] - width, cells.shape[dim], axis=dim)
    return jnp.concatenate(
        [
            lax.ppermute(tail, axis, [(i, (i + 1) % count) for i in range(ends)]),
            cells,
            lax.ppermute(head, axis, [((i + 1) % count, i) for i in range(ends)]),
        ],
        axis=dim,
    )


def local(tile_sums, tile_dest, tile_place, tile_count):
    slot_count, fields, cells = tile_sums.shape
    planes = cells // (TE * TE)
    across = lax.axis_size("gx")
    column_count = lax.axis_size("gy")
    peer_count = across * column_count
    is_live = jnp.arange(slot_count, dtype=jnp.int32) < tile_count[0]
    targets = jnp.arange(peer_count, dtype=jnp.int32)
    chosen = tile_dest[None, :] == targets[:, None]
    pick = chosen.astype(jnp.bfloat16)
    out_place = jnp.sum(jnp.where(chosen & is_live[None, :], tile_place[None, :] + 1, 0), axis=1) - 1

    def send(f):
        record = tile_sums[:, f, :]
        outgoing = jnp.dot(pick, record, preferred_element_type=jnp.float32).astype(jnp.bfloat16)
        outgoing = outgoing.reshape(peer_count, rows, 128)
        if f == 0:
            marks = jnp.broadcast_to(out_place.astype(jnp.bfloat16)[:, None, None], (peer_count, 8, 128))
            outgoing = jnp.concatenate([outgoing, marks], axis=1)
        return lax.all_to_all(outgoing, ("gx", "gy"), 0, 0, tiled=True)

    rows = cells // 128
    incoming = send(0)
    in_place = incoming[:, rows, 0].astype(jnp.int32)
    incoming = incoming[:, :rows]
    local_ids = jnp.arange(BX * BY, dtype=jnp.int32)
    landing = (in_place[None, :] == local_ids[:, None]).astype(jnp.bfloat16)
    height = BY * TE
    width = BX * TE
    wz = band(planes, planes, 0)
    wy = band(height + 2 * RADIUS, height, RADIUS)
    rows = cells // 128

    def proc(incoming):
        deposited = jnp.einsum("ts,src->trc", landing, incoming, preferred_element_type=jnp.float32)
        deposited = deposited.reshape(BY, BX, planes, TE, TE).transpose(2, 0, 3, 1, 4)
        deposited = deposited.reshape(planes, height, width)
        along_z = jnp.einsum("io,iyx->oyx", wz, deposited, precision=HIGHEST)
        padded = halo(along_z, "gy", 1, RADIUS)
        return jnp.einsum("iy,zix->zxy", wy, padded, precision=HIGHEST)

    def gather_x(along_y):
        return lax.all_to_all(along_y, "gx", 1, 1, tiled=True)

    def spread_x(along_y):
        me_x = lax.axis_index("gx")
        pieces = [lax.dynamic_slice_in_dim(along_y, me_x, 1, axis=0)]
        for shift in range(1, across):
            piece = lax.dynamic_slice_in_dim(along_y, (me_x + shift) % across, 1, axis=0)
            pieces.append(lax.ppermute(piece, "gx", [(g, (g + shift) % across) for g in range(across)]))
        stacked = jnp.concatenate(pieces, axis=0)
        order = (me_x - jnp.arange(across, dtype=jnp.int32)) % across
        return jnp.take(stacked, order, axis=0)[None]

    def along_x(blocks):
        count = blocks.shape[0]
        edge = jnp.zeros((count, 1, width, height), blocks.dtype)
        padded = jnp.concatenate([edge, blocks, edge], axis=1)
        result = jnp.einsum("fjxy,xo->fyjo", padded[:, 1 : across + 1], w_mid, precision=HIGHEST)
        reach = width - RADIUS
        from_left = jnp.einsum("fjxy,xo->fyjo", padded[:, 0:across, reach:], w_left[reach:, :RADIUS], precision=HIGHEST)
        from_right = jnp.einsum(
            "fjxy,xo->fyjo", padded[:, 2 : across + 2, :RADIUS], w_right[:RADIUS, reach:], precision=HIGHEST
        )
        zeros = jnp.zeros(from_left.shape[:3] + (reach,), result.dtype)
        result = result + jnp.concatenate([from_left, zeros], axis=3) + jnp.concatenate([zeros, from_right], axis=3)
        return result.reshape(count, 1, height, across * width)

    w_mid = band(width, width, 0)
    w_left = band(width, width, width)
    w_right = band(width, width, -width)
    smoothed = []
    for f in range(fields - 1):
        following = send(f + 1)
        smoothed.append(proc(incoming))
        incoming = following
    early = spread_x(smoothed.pop())
    first = gather_x(jnp.stack(smoothed, axis=0))
    last = proc(incoming)
    last = spread_x(last)
    spare = jnp.zeros((2,) + first.shape[1:], first.dtype)
    result = along_x(jnp.concatenate([first, spare], axis=0))
    return lax.dynamic_update_slice_in_dim(result, along_x(jnp.concatenate([early, last], axis=0)), fields - 2, axis=0)


def solution(mesh):
    return jax.shard_map(
        local,
        mesh=mesh,
        in_specs=(P(("gx", "gy"), None, None), P(("gx", "gy")), P(("gx", "gy")), P(("gx", "gy"))),
        out_specs=P(None, "gx", "gy", None),
        check_vma=False,
    )
```

```python
import math

import jax
import jax.numpy as jnp
import numpy as np
from jax import lax
from jax.sharding import PartitionSpec as P

TE = 32
BX = 4
BY = 4
RADIUS = 4
HIGHEST = lax.Precision.HIGHEST


def gauss_taps():
    spread = RADIUS * 5.0 / 16.0
    raw_taps = [
        math.exp(-(offset * offset) / (2.0 * spread * spread))
        for offset in range(-RADIUS, RADIUS + 1)
    ]
    total_weight = sum(raw_taps)
    return [value / total_weight for value in raw_taps]


def band(length_in, length_out, shift):
    taps = gauss_taps()
    mat = np.zeros((length_in, length_out), np.float32)
    for j in range(length_out):
        for k in range(2 * RADIUS + 1):
            i = j + shift + k - RADIUS
            if 0 <= i < length_in:
                mat[i, j] = taps[k]
    return jnp.asarray(mat)


def halo(cells, axis, dim, width):
    count = lax.axis_size(axis)
    ends = count - 1
    head = lax.slice_in_dim(cells, 0, width, axis=dim)
    tail = lax.slice_in_dim(cells, cells.shape[dim] - width, cells.shape[dim], axis=dim)
    return jnp.concatenate(
        [
            lax.ppermute(tail, axis, [(i, (i + 1) % count) for i in range(ends)]),
            cells,
            lax.ppermute(head, axis, [((i + 1) % count, i) for i in range(ends)]),
        ],
        axis=dim,
    )


def local(tile_sums, tile_dest, tile_place, tile_count):
    slot_count, fields, cells = tile_sums.shape
    planes = cells // (TE * TE)
    across = lax.axis_size("gx")
    column_count = lax.axis_size("gy")
    peer_count = across * column_count
    is_live = jnp.arange(slot_count, dtype=jnp.int32) < tile_count[0]
    targets = jnp.arange(peer_count, dtype=jnp.int32)
    chosen = tile_dest[None, :] == targets[:, None]
    pick = chosen.astype(jnp.bfloat16)
    out_place = jnp.sum(jnp.where(chosen & is_live[None, :], tile_place[None, :] + 1, 0), axis=1) - 1

    def send(f):
        record = tile_sums[:, f, :]
        outgoing = jnp.dot(pick, record, preferred_element_type=jnp.float32).astype(jnp.bfloat16)
        outgoing = outgoing.reshape(peer_count, rows, 128)
        if f == 0:
            marks = jnp.broadcast_to(out_place.astype(jnp.bfloat16)[:, None, None], (peer_count, 8, 128))
            outgoing = jnp.concatenate([outgoing, marks], axis=1)
        return lax.all_to_all(outgoing, ("gx", "gy"), 0, 0, tiled=True)

    rows = cells // 128
    incoming = send(0)
    in_place = incoming[:, rows, 0].astype(jnp.int32)
    incoming = incoming[:, :rows]
    local_ids = jnp.arange(BX * BY, dtype=jnp.int32)
    landing = (in_place[None, :] == local_ids[:, None]).astype(jnp.bfloat16)
    height = BY * TE
    width = BX * TE
    wz = band(planes, planes, 0)
    wy = band(height + 2 * RADIUS, height, RADIUS)
    rows = cells // 128

    def proc(incoming):
        deposited = jnp.einsum("ts,src->trc", landing, incoming, preferred_element_type=jnp.float32)
        deposited = deposited.reshape(BY, BX, planes, TE, TE).transpose(2, 0, 3, 1, 4)
        deposited = deposited.reshape(planes, height, width)
        along_z = jnp.einsum("io,iyx->oyx", wz, deposited, precision=HIGHEST)
        padded = halo(along_z, "gy", 1, RADIUS)
        return jnp.einsum("iy,zix->zxy", wy, padded, precision=HIGHEST)

    def gather_x(along_y):
        return lax.all_to_all(along_y, "gx", 1, 1, tiled=True)

    def spread_x(along_y):
        me_x = lax.axis_index("gx")
        pieces = [lax.dynamic_slice_in_dim(along_y, me_x, 1, axis=0)]
        for shift in range(1, across):
            piece = lax.dynamic_slice_in_dim(along_y, (me_x + shift) % across, 1, axis=0)
            pieces.append(lax.ppermute(piece, "gx", [(g, (g + shift) % across) for g in range(across)]))
        stacked = jnp.concatenate(pieces, axis=0)
        order = (me_x - jnp.arange(across, dtype=jnp.int32)) % across
        return jnp.take(stacked, order, axis=0)[None]

    def along_x(blocks):
        count = blocks.shape[0]
        edge = jnp.zeros((count, 1, width, height), blocks.dtype)
        padded = jnp.concatenate([edge, blocks, edge], axis=1)
        result = jnp.einsum("fjxy,xo->fyjo", padded[:, 1 : across + 1], w_mid, precision=HIGHEST)
        reach = width - RADIUS
        from_left = jnp.sum(
            padded[:, 0:across, reach:, :, None] * w_left[reach:, :RADIUS][:, None, :], axis=2
        ).transpose(0, 2, 1, 3)
        from_right = jnp.sum(
            padded[:, 2 : across + 2, :RADIUS, :, None] * w_right[:RADIUS, reach:][:, None, :], axis=2
        ).transpose(0, 2, 1, 3)
        zeros = jnp.zeros(from_left.shape[:3] + (reach,), result.dtype)
        result = result + jnp.concatenate([from_left, zeros], axis=3) + jnp.concatenate([zeros, from_right], axis=3)
        return result.reshape(count, 1, height, across * width)

    w_mid = band(width, width, 0)
    w_left = band(width, width, width)
    w_right = band(width, width, -width)
    smoothed = []
    for f in range(fields - 1):
        following = send(f + 1)
        smoothed.append(proc(incoming))
        incoming = following
    first = gather_x(jnp.stack(smoothed, axis=0))
    last = proc(incoming)
    last = spread_x(last)
    spare = jnp.zeros((1,) + first.shape[1:], first.dtype)
    result = along_x(jnp.concatenate([first, spare], axis=0))
    return lax.dynamic_update_slice_in_dim(result, along_x(last), fields - 1, axis=0)


def solution(mesh):
    return jax.shard_map(
        local,
        mesh=mesh,
        in_specs=(P(("gx", "gy"), None, None), P(("gx", "gy")), P(("gx", "gy")), P(("gx", "gy"))),
        out_specs=P(None, "gx", "gy", None),
        check_vma=False,
    )
```
